256 devices in a mesh: seq: 32 (over y, z), tensor: 8 (over x, core).
Axes of the slice: x: 4, y: 4, z: 8, core: 2. Of those that a mesh axis runs over, the one named last changes fastest.
Arguments:
- query: bfloat16 [4096, 2048], P('seq', 'tensor')
- suffix_kv: bfloat16 [4096, 4, 2, 128], P('seq'), may hold values from -6 to 6
- segment_ids: int32 [32, 128], P('seq'), may hold values from 0 to 3, never falling along the last dimension, each value on 1 to 64 neighbouring positions
- request_prefix: int32 [32, 4], P('seq'), may hold values from 0 to 3
- prefix_kv: bfloat16 [32768, 4, 2, 128], P('seq')
- shard_prefix: int32 [32], P('seq'), may hold values from 0 to 3, as said below
- residual: bfloat16 [4096, 2048], P('seq'), may hold values from -3.2 to 3.2
- out_weight: bfloat16 [2048, 2048], P('tensor'), may hold values from -0.1875 to 0.1875
- norm_gain: float32 [2048], replicated, may hold values from 0.1 to 1.9
- expert_ids: int32 [4096, 6], P('seq'), may hold values from 0 to 63, all different within a row; in each aligned block of 128 rows (0 to 127, 128 to 255, ...) at most 24 rows name the same one
- gate_weights: float32 [4096, 6], P('seq'), may hold values from 0.05 to 0.5
- expert_in: bfloat16 [64, 2048, 2, 1408], P('seq', None, None, 'tensor'), may hold values from -0.125 to 0.125
- expert_out: bfloat16 [64, 1408, 2048], P('seq', 'tensor'), may hold values from -0.21875 to 0.21875
Outputs:
- attended: bfloat16 [4096, 2048], P('seq', 'tensor')
- layer_out: bfloat16 [4096, 2048], P('seq', 'tensor')
The draws below stay inside these ranges and needn't reach their ends.
Inputs may be any that keep to these rules, and one draw needn't show every extreme that they name: `segment_ids`: on each seq index the segment numbers never fall along the 128 positions and every number occurs. `shard_prefix`: every prefix owns the same number of shards. `expert_ids`: each row names 6 different experts; within the 128 rows of one seq index no expert is named more than 24 times, and that count is reached.
All inputs are finite; a program needn't handle non-finite values.
Results may differ from the reference program's by a relative error of at most 0.02.
Values may be sent and summed in bfloat16 or wider, within the bound.
No kernel may reach another device: no remote copies, remote signals or barrier semaphores. Data moves between devices by JAX's collectives and lax.ppermute only.
A program may use at most 128 MiB of HBM per device.

```python
import math
import jax
import jax.numpy as jnp
import numpy as np
from jax import lax

D = 2048
QH = 16
KVH = 4
HD = 128
MOE_FF = 1408
TOP = 6
PREFIXES = 4
REQ_DEV = 4
TOK_DEV = 128
PSH = 1024
TOKENS = 4096
PREF_TOTAL = 32768
EXPERTS = 64
CAP = 24
HID_GROUP = 176
N_SEQ = 32
N_TENSOR = 8


def draw_query(key, part):
    shape = (TOKENS, QH * HD)
    base = jnp.clip(2.0 * jax.random.normal(jax.random.fold_in(key, 1), shape, jnp.float32), -8.0, 8.0)
    return base.astype(jnp.bfloat16)


def draw_prefix_kv(key, part):
    shape = (PREF_TOTAL, KVH, 2, HD)
    base = jnp.clip(jax.random.normal(jax.random.fold_in(key, 2), shape, jnp.float32), -6.0, 6.0)
    return base.astype(jnp.bfloat16)


def draw_shard_prefix(key, part):
    shard_total = PREF_TOTAL // PSH
    order = jax.random.permutation(jax.random.fold_in(key, 3), shard_total)
    return (order // (shard_total // PREFIXES)).astype(jnp.int32)


def draw_residual(key, part):
    shape = (TOKENS, D)
    columns = jnp.arange(D).astype(jnp.float32) / D
    scale = 0.08 * 10.0 ** columns
    base = jnp.clip(jax.random.normal(jax.random.fold_in(key, 5), shape, jnp.float32), -4.0, 4.0)
    return (base * scale[None, :]).astype(jnp.bfloat16)


def set_ends(entries, stream_key, low, high):
    spot = [jax.random.randint(jax.random.fold_in(stream_key, axis), (), 0, length) for axis, length in enumerate(entries.shape)]
    main_axis = entries.shape.index(max(entries.shape))
    neighbour = spot[:main_axis] + [(spot[main_axis] + 1) % entries.shape[main_axis]] + spot[main_axis + 1:]
    return entries.at[tuple(spot)].set(low).at[tuple(neighbour)].set(high)


def strengthened(values, stream_key, source, target, blocks, factor):
    def block_of(dim):
        return (jnp.arange(values.shape[dim]) // (values.shape[dim] // blocks)).reshape((-1,) + (1,) * (values.ndim - 1 - dim))

    first = jax.random.permutation(stream_key, blocks)[block_of(target)]
    second = (block_of(target) + blocks // 2) % blocks
    return jnp.where((block_of(source) == first) | (block_of(source) == second), factor * values, values)


def block_levels(rng, shape, pieces, low, high):
    def one(axis_at, shards_of):
        steps = jax.random.uniform(jax.random.fold_in(jax.random.fold_in(rng, 6), axis_at), (shards_of,), jnp.float32, low / len(pieces), high / len(pieces))
        return jnp.repeat(jnp.exp(steps), shape[axis_at] // shards_of).reshape((-1,) + (1,) * (len(shape) - axis_at - 1))

    gain = one(*pieces[0])
    for cut in pieces[1:]:
        gain = gain * one(*cut)
    return gain


def rank_bounds(number_of, lean):
    loads = [(1 << 20) // math.isqrt(standing ** lean) + 1 for standing in range(1, number_of + 1)]
    deviation = 1 + sum(loads) // (1 << 30)
    return np.cumsum(np.array([max(1, weight // deviation) for weight in loads]))


def skewed_ids(stream_key, dims, number_of, lean):
    table = rank_bounds(number_of, lean)
    ticket = jax.random.randint(jax.random.fold_in(stream_key, 1), dims, 0, int(table[number_of - 1]))
    grade = jnp.searchsorted(jnp.asarray(table, jnp.int32), ticket, side="right")
    return jax.random.permutation(jax.random.fold_in(stream_key, 2), number_of)[grade].astype(jnp.int32)


def length_profile(amount, total, most, slope):
    loads = [(1 << 20) // math.isqrt(grade ** slope) + 1 for grade in range(2, amount + 1)]
    surplus, given = total - most - (amount - 1), [1] * (amount - 1)
    while surplus > 0:
        free = [i for i in range(amount - 1) if given[i] < most]
        pool, remaining = sum([loads[i] for i in free]), surplus
        for i in free:
            more = min(most - given[i], max(1, remaining * loads[i] // pool), surplus)
            given[i] = given[i] + more
            surplus = surplus - more
    return np.array([most] + given)


def uneven_parts(stream_key, amount, total, most, slope):
    if amount == 2:
        one = jax.random.randint(stream_key, (), max(1, total - most), min(most, total - 1) + 1)
        return jnp.stack([one, total - one])
    sizes = jnp.asarray(length_profile(amount, total, most, slope), jnp.int32)
    twos = (amount - 1) // 2
    giver, sink = sizes[1:1 + 2 * twos:2], sizes[2:2 + 2 * twos:2]
    margin = jnp.minimum(giver - 1, most - sink)
    shifted = jax.random.randint(jax.random.fold_in(stream_key, 1), (twos,), 0, 1 << 20) % (margin + 1)
    sizes = sizes.at[1:1 + 2 * twos:2].set(giver - shifted).at[2:2 + 2 * twos:2].set(sink + shifted)
    return sizes[jax.random.permutation(jax.random.fold_in(stream_key, 2), amount)]


def routed_block(own_key, own, number, rows, amount, top, most, lean):
    order = jax.random.permutation(own_key, amount)
    crowded, common = shares(amount, rows * top, most, lean, True), shares(amount, rows * top, most, lean, False)
    places = jnp.arange(amount)

    def named(lengths, offset_by):
        used = int((lengths > 0).sum())
        fixed = max(1, used // 4)
        passed = fixed + (places - fixed + offset_by * (used - fixed)) % max(1, amount - fixed)
        return jnp.zeros((amount,), jnp.int32).at[order[jnp.where(places < fixed, places, passed)]].set(jnp.asarray(lengths, jnp.int32))

    lengths = jnp.where(number % 4 == 0, named(crowded, number // 4), named(common, number - number // 4 - 1))
    mixed = jax.random.permutation(jax.random.fold_in(own, 3), amount)
    source_of, sink = mixed[0:amount // 2 * 2:2], mixed[1:amount // 2 * 2:2]
    room = jnp.minimum(lengths[source_of] - 1, most - lengths[sink]) // 2
    room = jnp.where((source_of == order[0]) | (sink == order[0]) | (lengths[sink] == 0), 0, jnp.maximum(room, 0))
    passed = jax.random.randint(jax.random.fold_in(own, 4), (amount // 2,), 0, 1 << 20) % (room + 1)
    lengths = lengths.at[source_of].add(-passed).at[sink].add(passed)
    items = jnp.searchsorted(jnp.cumsum(lengths), jnp.arange(rows * top), side="right").astype(jnp.int32)
    listing = items.reshape(top, rows).T
    listing = listing[jax.random.permutation(jax.random.fold_in(own, 1), rows)]
    offset_by = jax.random.randint(jax.random.fold_in(own, 2), (rows, 1), 0, top)
    return jnp.take_along_axis(listing, (jnp.arange(top)[None, :] + offset_by) % top, axis=1)


def shares(amount, total, most, skew, full):
    weights = [(1 << 20) // math.isqrt(standing ** skew) + 1 for standing in range(1, amount + 1)]
    largest = most if full else min(most, max(-(-total // amount), total * weights[0] // sum(weights)))
    least = 1 if total - largest >= amount - 1 else 0
    given, spare = [largest] + [least] * (amount - 1), total - largest - least * (amount - 1)
    while spare > 0:
        candidates = [i for i in range(1, amount) if given[i] < largest] or [i for i in range(1, amount) if given[i] < most]
        pool, left = sum([weights[i] for i in candidates]), spare
        for i in candidates:
            more = min(most - given[i], max(1, left * weights[i] // pool), spare)
            given[i] = given[i] + more
            spare = spare - more
    return np.array(given)


def normal_values(key, extent, spread, bound, shards=(), held_as=jnp.bfloat16):
    values = jax.random.normal(key, extent, jnp.float32) * spread
    if len(shards) > 0:
        values = block_levels(key, extent, shards, -0.22, 0.18) * values
    return jnp.clip(values, min=-bound, max=bound).astype(held_as)


def bell_draw_with(rng, shape, scale, bound, pieces, heavy, kind=jnp.bfloat16):
    entries = scale * jax.random.normal(rng, shape, jnp.float32)
    if pieces:
        entries = entries * block_levels(rng, shape, pieces, -0.22, 0.18)
    return jnp.clip(strengthened(entries, jax.random.fold_in(rng, 3), *heavy), -bound, bound).astype(kind)


def setup_inputs(seed: int = 0) -> dict:
    arg_keys = jax.random.split(jax.random.key(seed), 14)
    query = draw_query(jax.random.fold_in(arg_keys[13], 71), 0)
    suffix_kv = normal_values(arg_keys[1], (TOKENS, KVH, 2, HD), 1.0, 6.0, ((0, 32),))
    segment_ids = jax.vmap(lambda own: jnp.searchsorted(jnp.cumsum(uneven_parts(own, REQ_DEV, TOK_DEV, TOK_DEV // 2, 1)), jnp.arange(TOK_DEV), side="right"))(jax.random.split(arg_keys[2], N_SEQ)).reshape((N_SEQ, TOK_DEV)).astype(jnp.int32)
    request_prefix = set_ends(skewed_ids(arg_keys[3], (N_SEQ, REQ_DEV), PREFIXES, 2), jax.random.fold_in(arg_keys[3], 3), 0, PREFIXES - 1).astype(jnp.int32)
    prefix_kv = draw_prefix_kv(jax.random.fold_in(arg_keys[13], 71), 0)
    shard_prefix = draw_shard_prefix(jax.random.fold_in(arg_keys[13], 71), 0)
    residual = draw_residual(jax.random.fold_in(arg_keys[13], 71), 0)
    out_weight = bell_draw_with(arg_keys[7], (QH * HD, D), (QH * HD) ** -0.5, 0.1875, ((0, 8),), (0, 1, 8, 2.0))
    norm_gain = jnp.clip(1.0 + 0.18 * jax.random.normal(arg_keys[8], (D,), jnp.float32), 0.1, 1.9)
    expert_ids_keys = jax.random.split(jax.random.fold_in(arg_keys[9], 1), TOKENS // TOK_DEV)
    expert_ids_turns = jax.random.permutation(jax.random.fold_in(arg_keys[9], 3), TOKENS // TOK_DEV)
    expert_ids = jax.vmap(lambda own, number: routed_block(jax.random.fold_in(arg_keys[9], 2), own, number, TOK_DEV, EXPERTS, TOP, CAP, 2))(expert_ids_keys, expert_ids_turns).reshape((TOKENS, TOP))
    gate_weights = jnp.clip(jnp.exp(math.log(0.5) - 2.3025851 * jax.random.uniform(arg_keys[10], (TOKENS, TOP), jnp.float32) ** block_levels(arg_keys[10], (TOKENS, TOP), ((0, 32),), -0.2, 0.2)), 0.05, 0.5)
    expert_in = normal_values(arg_keys[11], (EXPERTS, D, 2, MOE_FF), D ** -0.5, 0.125, ((0, 32), (3, 8)))
    expert_out = bell_draw_with(arg_keys[12], (EXPERTS, MOE_FF, D), MOE_FF ** -0.5, 0.21875, ((0, 32), (1, 8)), (1, 2, 8, 2.0))
    return dict(query=query, suffix_kv=suffix_kv, segment_ids=segment_ids, request_prefix=request_prefix, prefix_kv=prefix_kv, shard_prefix=shard_prefix, residual=residual, out_weight=out_weight, norm_gain=norm_gain, expert_ids=expert_ids, gate_weights=gate_weights, expert_in=expert_in, expert_out=expert_out)


PRECISE = lax.Precision.HIGHEST

def rounded(values):
    return lax.optimization_barrier(values.astype(jnp.bfloat16)).astype(jnp.float32)

def attend_device(device_item, prefix_kv, key_owner):
    queries, suffix_rows, segments, requests = device_item
    groups = QH // KVH
    query_f32 = queries.astype(jnp.float32).reshape(TOK_DEV, KVH, groups, HD)
    prefix_f32 = prefix_kv.astype(jnp.float32)
    suffix_f32 = suffix_rows.astype(jnp.float32)
    score_scale = HD ** (-0.5)
    row_prefix = requests[segments]
    prefix_scores = jnp.einsum('tkgd,pkd->kgtp', query_f32, prefix_f32[:, :, 0], precision=PRECISE) * score_scale
    visible = row_prefix[:, None] == key_owner[None, :]
    prefix_scores = jnp.where(visible[None, None], prefix_scores, -jnp.inf)
    positions = jnp.arange(TOK_DEV)
    causal = (segments[:, None] == segments[None, :]) & (positions[None, :] <= positions[:, None])
    suffix_scores = jnp.einsum('tkgd,skd->kgts', query_f32, suffix_f32[:, :, 0], precision=PRECISE) * score_scale
    suffix_scores = jnp.where(causal[None, None], suffix_scores, -jnp.inf)
    highest = jnp.maximum(lax.optimization_barrier(jnp.max(prefix_scores, axis=3)), lax.optimization_barrier(jnp.max(suffix_scores, axis=3)))
    prefix_weights = jnp.exp(prefix_scores - highest[..., None])
    suffix_weights = jnp.exp(suffix_scores - highest[..., None])
    denominator = lax.optimization_barrier(jnp.sum(prefix_weights, axis=3)) + lax.optimization_barrier(jnp.sum(suffix_weights, axis=3))
    combined = jnp.einsum('kgtp,pkd->tkgd', rounded(prefix_weights), prefix_f32[:, :, 1], precision=PRECISE)
    combined = combined + jnp.einsum('kgts,skd->tkgd', rounded(suffix_weights), suffix_f32[:, :, 1], precision=PRECISE)
    combined = combined / jnp.transpose(denominator, (2, 0, 1))[..., None]
    return combined.reshape(TOK_DEV, QH * HD).astype(jnp.bfloat16)

def run_expert(expert_item):
    rows_in, weight_in, weight_out = expert_item
    gate_up = jnp.dot(rows_in, weight_in.reshape(D, 2 * MOE_FF), preferred_element_type=jnp.float32)
    gate_up = gate_up.reshape(-1, 2, MOE_FF)
    hidden = (jax.nn.silu(gate_up[:, 0]) * gate_up[:, 1]).astype(jnp.bfloat16)
    grouped = jnp.einsum('rgh,ghd->grd', hidden.reshape(-1, N_TENSOR, HID_GROUP).astype(jnp.float32), weight_out.reshape(N_TENSOR, HID_GROUP, D).astype(jnp.float32), precision=PRECISE)
    grouped = lax.optimization_barrier(grouped.astype(jnp.bfloat16))
    return lax.optimization_barrier(jnp.sum(grouped.astype(jnp.float32), axis=0)).astype(jnp.bfloat16)

def reference(query, suffix_kv, segment_ids, request_prefix, prefix_kv, shard_prefix, residual, out_weight, norm_gain, expert_ids, gate_weights, expert_in, expert_out):
    key_owner = jnp.repeat(shard_prefix, PSH)

    def one_device(device_item):
        return attend_device(device_item, prefix_kv, key_owner)
    attention = lax.map(one_device, (query.reshape(N_SEQ, TOK_DEV, QH * HD), suffix_kv.reshape(N_SEQ, TOK_DEV, KVH, 2, HD), segment_ids, request_prefix))
    attention = attention.reshape(TOKENS, QH * HD)
    hidden_state = residual.astype(jnp.float32) + jnp.dot(attention, out_weight, preferred_element_type=jnp.float32)
    attended = hidden_state.astype(jnp.bfloat16)
    mean_square = lax.optimization_barrier(jnp.mean(hidden_state * hidden_state, axis=1, keepdims=True))
    normed = (hidden_state * lax.rsqrt(mean_square + 1e-06) * norm_gain.astype(jnp.float32)[None, :]).astype(jnp.bfloat16)
    flat_ids = expert_ids.reshape(N_SEQ, TOK_DEV * TOP).astype(jnp.int32)
    onehot = (flat_ids[:, :, None] == jnp.arange(EXPERTS, dtype=jnp.int32)[None, None, :]).astype(jnp.int32)
    slot_index = lax.optimization_barrier(jnp.sum((jnp.cumsum(onehot, axis=1) - 1) * onehot, axis=2)).astype(jnp.int32)
    sources = jnp.arange(N_SEQ, dtype=jnp.int32)[:, None]
    places = ((flat_ids * N_SEQ + sources) * CAP + slot_index).reshape(-1).astype(jnp.int32)
    table = jnp.zeros((EXPERTS * N_SEQ * CAP, D), jnp.bfloat16).at[places].set(jnp.repeat(normed, TOP, axis=0))
    table = table.reshape(EXPERTS, N_SEQ * CAP, D)
    outputs = lax.map(run_expert, (table, expert_in, expert_out))
    picked = outputs.reshape(EXPERTS * N_SEQ * CAP, D)[places].reshape(TOKENS, TOP, D)
    mixture = lax.optimization_barrier(jnp.sum(gate_weights[:, :, None] * picked.astype(jnp.float32), axis=1))
    layer_out = (hidden_state + mixture).astype(jnp.bfloat16)
    return (attended, layer_out)
```

```python
import functools

import jax
import jax.numpy as jnp
from jax import lax
from jax.experimental import pallas as pl
from jax.experimental.pallas import tpu as pltpu
from jax.sharding import PartitionSpec as P

QH = 16
KVH = 4


NEG_FLOOR = -1e30
NEG_SHIFT = -(2.0 ** 100)
TOKEN_BLOCKS = 4


def split3(x):
    hi = x.astype(jnp.bfloat16).astype(jnp.float32)
    rest = x - hi
    mid = rest.astype(jnp.bfloat16).astype(jnp.float32)
    lo = (rest - mid).astype(jnp.bfloat16).astype(jnp.float32)
    return hi, mid, lo


def shard_kernel(q_ref, k_ref, v_ref, o_ref, st_ref, *, score_scale):
    blocks, rows, width = q_ref.shape
    q = q_ref[...].reshape(blocks * rows, width)
    scores = (
        lax.dot_general(
            q, k_ref[...], (((1,), (1,)), ((), ())), preferred_element_type=jnp.float32
        )
        * score_scale
    )
    shift = jnp.max(scores, axis=1, keepdims=True)
    weights = jnp.exp(scores - shift)
    total = jnp.sum(weights, axis=1, keepdims=True)
    gathered = jnp.dot(
        weights.astype(jnp.bfloat16), v_ref[...], preferred_element_type=jnp.float32
    )
    o_ref[...] = gathered.astype(jnp.bfloat16).reshape(blocks, 1, rows, width)
    parts = split3(shift) + split3(total)
    for col, part in enumerate(parts):
        st_ref[0, :, col : col + 1] = part
    st_ref[0, :, 6:8] = jnp.zeros((blocks * rows, 2), jnp.float32)


def shard_attention(gathered_q, keys, values, score_scale):
    sources, padded_rows, two_heads = gathered_q.shape
    head_size = keys.shape[1]
    rows = padded_rows - 1
    heads = two_heads // head_size
    tb = TOKEN_BLOCKS
    kernel = functools.partial(shard_kernel, score_scale=score_scale)
    return pl.pallas_call(
        kernel,
        grid=(sources // tb, heads),
        in_specs=[
            pl.BlockSpec((tb, rows, head_size), lambda b, h: (b, 0, h)),
            pl.BlockSpec(keys.shape, lambda b, h: (0, 0)),
            pl.BlockSpec(values.shape, lambda b, h: (0, 0)),
        ],
        out_specs=[
            pl.BlockSpec((tb, 1, rows, head_size), lambda b, h: (b, h, 0, 0)),
            pl.BlockSpec((1, tb * rows, 8), lambda b, h: (h, b, 0)),
        ],
        out_shape=[
            jax.ShapeDtypeStruct((sources, heads, rows, head_size), jnp.bfloat16),
            jax.ShapeDtypeStruct((heads, sources * rows, 8), jnp.float32),
        ],
    )(gathered_q, keys, values)


def body(
    query,
    suffix_kv,
    segment_ids,
    request_prefix,
    prefix_kv,
    shard_prefix,
    residual,
    out_weight,
    norm_gain,
    expert_ids,
    gate_weights,
    expert_in,
    expert_out,
):
    tok_rows = query.shape[0]
    head_size = suffix_kv.shape[3]
    heads_here = query.shape[1] // head_size
    kv_head = lax.axis_index("tensor") * heads_here // (QH // KVH)
    score_scale = head_size ** (-0.5)
    queries = query.reshape(tok_rows, heads_here, head_size)
    segments = segment_ids[0]
    requests = jnp.arange(request_prefix.shape[1], dtype=jnp.int32)
    row_prefix = jnp.sum(
        jnp.where(segments[:, None] == requests[None, :], request_prefix[0][None, :], 0), axis=1
    )
    prefix_row = jnp.zeros((1, query.shape[1]), jnp.bfloat16).at[0, :tok_rows].set(
        row_prefix.astype(jnp.bfloat16)
    )
    gathered_q = lax.all_gather(
        jnp.concatenate([query, prefix_row], axis=0), "seq", axis=0, tiled=False
    )
    sources = gathered_q.shape[0]
    own_cache = lax.dynamic_slice_in_dim(prefix_kv, kv_head, 1, 1)[:, 0]
    part_o, part_st = shard_attention(
        gathered_q, own_cache[:, 0], own_cache[:, 1], score_scale
    )
    valid = gathered_q[:, tok_rows, :tok_rows] == shard_prefix[0].astype(jnp.bfloat16)
    stats = part_st.reshape(heads_here, sources, tok_rows, 8)
    keep = valid[None, :, :, None]
    column = jnp.arange(8)[None, None, None, :]
    stats = jnp.where(keep, stats, jnp.where(column == 0, NEG_SHIFT, 0.0))
    stats = jnp.transpose(stats, (1, 0, 3, 2)).astype(jnp.bfloat16)
    outgoing = jnp.concatenate([part_o, stats], axis=2)
    returned = lax.all_to_all(outgoing, "seq", split_axis=0, concat_axis=0, tiled=True)
    got_o = returned[:, :, :tok_rows, :].astype(jnp.float32)
    got_st = returned[:, :, tok_rows:, :].astype(jnp.float32)
    got_shift = got_st[:, :, 0] + got_st[:, :, 1] + got_st[:, :, 2]
    got_total = got_st[:, :, 3] + got_st[:, :, 4] + got_st[:, :, 5]

    own_suffix = lax.dynamic_slice_in_dim(suffix_kv, kv_head, 1, 1).reshape(tok_rows, 2, head_size)
    positions = jnp.arange(tok_rows)
    causal = (segments[:, None] == segments[None, :]) & (positions[None, :] <= positions[:, None])
    suf_scores = (
        jnp.einsum("rhd,kd->hrk", queries, own_suffix[:, 0], preferred_element_type=jnp.float32)
        * score_scale
    )
    suf_scores = jnp.where(causal[None], suf_scores, -jnp.inf)
    suf_shift = jnp.max(suf_scores, axis=2)
    suf_weights = jnp.exp(suf_scores - suf_shift[:, :, None])
    suf_total = jnp.sum(suf_weights, axis=2)
    suf_o = jnp.einsum(
        "hrk,kd->hrd", suf_weights.astype(jnp.bfloat16), own_suffix[:, 1],
        preferred_element_type=jnp.float32,
    )
    common = jnp.maximum(suf_shift, jnp.max(got_shift, axis=0))
    got_scale = jnp.exp(got_shift - common[None])
    suf_scale = jnp.exp(suf_shift - common)
    numer = jnp.sum(got_o * got_scale[..., None], axis=0) + suf_o * suf_scale[..., None]
    denom = jnp.sum(got_total * got_scale, axis=0) + suf_total * suf_scale
    attention = (
        jnp.transpose(numer / denom[..., None], (1, 0, 2))
        .reshape(tok_rows, heads_here * head_size)
        .astype(jnp.bfloat16)
    )
    projected = jnp.dot(attention, out_weight, preferred_element_type=jnp.float32)
    model_width = residual.shape[1]
    slice_width = model_width // lax.axis_size("tensor")
    first_col = lax.axis_index("tensor") * slice_width
    shared = lax.psum_scatter(projected, "tensor", scatter_dimension=1, tiled=True)
    hidden_state = (
        lax.dynamic_slice_in_dim(residual, first_col, slice_width, 1).astype(jnp.float32) + shared
    )
    squares = lax.psum(jnp.sum(hidden_state * hidden_state, axis=1), "tensor")
    gain_cols = lax.dynamic_slice_in_dim(norm_gain, first_col, slice_width, 0)
    normed = (
        hidden_state * lax.rsqrt(squares / model_width + 1e-06)[:, None] * gain_cols[None, :]
    ).astype(jnp.bfloat16)
    attended = hidden_state.astype(jnp.bfloat16)
    exp_here = expert_in.shape[0]
    sources = lax.axis_size("seq")
    experts = exp_here * sources
    top_k = expert_ids.shape[1]
    capacity = 2 * tok_rows * top_k // experts
    flat_ids = expert_ids.reshape(-1)
    onehot = (flat_ids[:, None] == jnp.arange(experts, dtype=jnp.int32)[None, :]).astype(jnp.int32)
    slot_index = jnp.sum((jnp.cumsum(onehot, axis=0) - 1) * onehot, axis=1)
    places = flat_ids * capacity + slot_index
    outgoing = (
        jnp.zeros((experts * capacity, slice_width), jnp.bfloat16)
        .at[places]
        .set(jnp.repeat(normed, top_k, axis=0))
    )
    incoming = lax.all_to_all(
        outgoing.reshape(sources, exp_here, capacity, slice_width),
        "seq",
        split_axis=0,
        concat_axis=0,
        tiled=True,
    )
    gate_up = jnp.einsum(
        "sjcd,jdgh->sjcgh",
        lax.all_gather(incoming, "tensor", axis=3, tiled=True),
        expert_in,
        preferred_element_type=jnp.float32,
    )
    hidden = (jax.nn.silu(gate_up[:, :, :, 0]) * gate_up[:, :, :, 1]).astype(jnp.bfloat16)
    group_terms = jnp.einsum(
        "sjch,jhd->sjcd", hidden, expert_out, preferred_element_type=jnp.float32
    )
    expert_rows_out = lax.psum_scatter(
        group_terms.astype(jnp.bfloat16), "tensor", scatter_dimension=3, tiled=True
    )
    returned = lax.all_to_all(expert_rows_out, "seq", split_axis=0, concat_axis=0, tiled=True)
    picked = returned.reshape(experts * capacity, slice_width)[places].reshape(
        tok_rows, top_k, slice_width
    )
    mixture = jnp.sum(gate_weights[:, :, None] * picked.astype(jnp.float32), axis=1)
    layer_out = (hidden_state + mixture).astype(jnp.bfloat16)
    return (attended, layer_out)


def solution(mesh):
    in_specs = (
        P("seq", "tensor"),
        P("seq", None, None, None),
        P("seq", None),
        P("seq", None),
        P("seq", None, None, None),
        P("seq"),
        P("seq", None),
        P("tensor", None),
        P(),
        P("seq", None),
        P("seq", None),
        P("seq", None, None, "tensor"),
        P("seq", "tensor", None),
    )
    out_specs = (P("seq", "tensor"), P("seq", "tensor"))
    return jax.shard_map(body, mesh=mesh, in_specs=in_specs, out_specs=out_specs, check_vma=False)
```

```python
import functools

import jax
import jax.numpy as jnp
from jax import lax
from jax.experimental import pallas as pl
from jax.experimental.pallas import tpu as pltpu
from jax.sharding import PartitionSpec as P

QH = 16
KVH = 4


NEG_FLOOR = -1e30
NEG_SHIFT = -(2.0 ** 100)
TOKEN_BLOCKS = 4


def split3(x):
    hi = x.astype(jnp.bfloat16).astype(jnp.float32)
    rest = x - hi
    mid = rest.astype(jnp.bfloat16).astype(jnp.float32)
    lo = (rest - mid).astype(jnp.bfloat16).astype(jnp.float32)
    return hi, mid, lo


def shard_kernel(flag_ref, q_ref, k_ref, v_ref, o_ref, st_ref, *, score_scale):
    step = pl.program_id(0)
    blocks, rows, width = q_ref.shape
    for i in range(blocks):
        present = flag_ref[step * blocks + i] > 0

        @pl.when(present)
        def _():
            scores = (
                lax.dot_general(
                    q_ref[i], k_ref[...], (((1,), (1,)), ((), ())),
                    preferred_element_type=jnp.float32,
                )
                * score_scale
            )
            shift = jnp.max(scores, axis=1, keepdims=True)
            weights = jnp.exp(scores - shift)
            total = jnp.sum(weights, axis=1, keepdims=True)
            gathered = jnp.dot(
                weights.astype(jnp.bfloat16), v_ref[...], preferred_element_type=jnp.float32
            )
            o_ref[i, 0] = gathered.astype(jnp.bfloat16)
            parts = split3(shift) + split3(total)
            for col, part in enumerate(parts):
                st_ref[0, i * rows : (i + 1) * rows, col : col + 1] = part
            st_ref[0, i * rows : (i + 1) * rows, 6:8] = jnp.zeros((rows, 2), jnp.float32)

        @pl.when(jnp.logical_not(present))
        def _():
            o_ref[i, 0] = jnp.zeros((rows, width), jnp.bfloat16)
            st_ref[0, i * rows : (i + 1) * rows, :] = jnp.zeros((rows, 8), jnp.float32)


def shard_attention(flags, gathered_q, keys, values, score_scale):
    sources, padded_rows, two_heads = gathered_q.shape
    head_size = keys.shape[1]
    rows = padded_rows - 1
    heads = two_heads // head_size
    tb = TOKEN_BLOCKS
    kernel = functools.partial(shard_kernel, score_scale=score_scale)
    grid_spec = pltpu.PrefetchScalarGridSpec(
        num_scalar_prefetch=1,
        grid=(sources // tb, heads),
        in_specs=[
            pl.BlockSpec((tb, rows, head_size), lambda b, h, f: (b, 0, h)),
            pl.BlockSpec(keys.shape, lambda b, h, f: (0, 0)),
            pl.BlockSpec(values.shape, lambda b, h, f: (0, 0)),
        ],
        out_specs=[
            pl.BlockSpec((tb, 1, rows, head_size), lambda b, h, f: (b, h, 0, 0)),
            pl.BlockSpec((1, tb * rows, 8), lambda b, h, f: (h, b, 0)),
        ],
    )
    return pl.pallas_call(
        kernel,
        grid_spec=grid_spec,
        out_shape=[
            jax.ShapeDtypeStruct((sources, heads, rows, head_size), jnp.bfloat16),
            jax.ShapeDtypeStruct((heads, sources * rows, 8), jnp.float32),
        ],
    )(flags, gathered_q, keys, values)


def body(
    query,
    suffix_kv,
    segment_ids,
    request_prefix,
    prefix_kv,
    shard_prefix,
    residual,
    out_weight,
    norm_gain,
    expert_ids,
    gate_weights,
    expert_in,
    expert_out,
):
    tok_rows = query.shape[0]
    head_size = suffix_kv.shape[3]
    heads_here = query.shape[1] // head_size
    kv_head = lax.axis_index("tensor") * heads_here // (QH // KVH)
    score_scale = head_size ** (-0.5)
    queries = query.reshape(tok_rows, heads_here, head_size)
    segments = segment_ids[0]
    requests = jnp.arange(request_prefix.shape[1], dtype=jnp.int32)
    row_prefix = jnp.sum(
        jnp.where(segments[:, None] == requests[None, :], request_prefix[0][None, :], 0), axis=1
    )
    prefix_row = jnp.zeros((1, query.shape[1]), jnp.bfloat16).at[0, :tok_rows].set(
        row_prefix.astype(jnp.bfloat16)
    )
    own_rows = jnp.concatenate([query, prefix_row], axis=0)
    sources = lax.axis_size("seq")
    gathered_q = lax.all_to_all(
        jnp.broadcast_to(own_rows[None], (sources,) + own_rows.shape),
        "seq", split_axis=0, concat_axis=0, tiled=True,
    )
    own_cache = lax.dynamic_slice_in_dim(prefix_kv, kv_head, 1, 1)[:, 0]
    valid = gathered_q[:, tok_rows, :tok_rows] == shard_prefix[0].astype(jnp.bfloat16)
    flags = jnp.any(valid, axis=1).astype(jnp.int32)
    part_o, part_st = shard_attention(
        flags, gathered_q, own_cache[:, 0], own_cache[:, 1], score_scale
    )
    stats = part_st.reshape(heads_here, sources, tok_rows, 8)
    keep = valid[None, :, :, None]
    column = jnp.arange(8)[None, None, None, :]
    stats = jnp.where(keep, stats, jnp.where(column == 0, NEG_SHIFT, 0.0))
    stats = jnp.transpose(stats, (1, 0, 3, 2)).astype(jnp.bfloat16)
    outgoing = jnp.concatenate([part_o, stats], axis=2)
    returned = lax.all_to_all(outgoing, "seq", split_axis=0, concat_axis=0, tiled=True)
    got_o = returned[:, :, :tok_rows, :].astype(jnp.float32)
    got_st = returned[:, :, tok_rows:, :].astype(jnp.float32)
    got_shift = got_st[:, :, 0] + got_st[:, :, 1] + got_st[:, :, 2]
    got_total = got_st[:, :, 3] + got_st[:, :, 4] + got_st[:, :, 5]

    own_suffix = lax.dynamic_slice_in_dim(suffix_kv, kv_head, 1, 1).reshape(tok_rows, 2, head_size)
    positions = jnp.arange(tok_rows)
    causal = (segments[:, None] == segments[None, :]) & (positions[None, :] <= positions[:, None])
    suf_scores = (
        jnp.einsum("rhd,kd->hrk", queries, own_suffix[:, 0], preferred_element_type=jnp.float32)
        * score_scale
    )
    suf_scores = jnp.where(causal[None], suf_scores, -jnp.inf)
    suf_shift = jnp.max(suf_scores, axis=2)
    suf_weights = jnp.exp(suf_scores - suf_shift[:, :, None])
    suf_total = jnp.sum(suf_weights, axis=2)
    suf_o = jnp.einsum(
        "hrk,kd->hrd", suf_weights.astype(jnp.bfloat16), own_suffix[:, 1],
        preferred_element_type=jnp.float32,
    )
    common = jnp.maximum(suf_shift, jnp.max(got_shift, axis=0))
    got_scale = jnp.exp(got_shift - common[None])
    suf_scale = jnp.exp(suf_shift - common)
    numer = jnp.sum(got_o * got_scale[..., None], axis=0) + suf_o * suf_scale[..., None]
    denom = jnp.sum(got_total * got_scale, axis=0) + suf_total * suf_scale
    attention = (
        jnp.transpose(numer / denom[..., None], (1, 0, 2))
        .reshape(tok_rows, heads_here * head_size)
        .astype(jnp.bfloat16)
    )
    projected = jnp.dot(attention, out_weight, preferred_element_type=jnp.float32)
    model_width = residual.shape[1]
    slice_width = model_width // lax.axis_size("tensor")
    first_col = lax.axis_index("tensor") * slice_width
    tensor_size = lax.axis_size("tensor")
    shared = jnp.sum(
        lax.all_to_all(
            projected.reshape(tok_rows, tensor_size, slice_width),
            "tensor", split_axis=1, concat_axis=1, tiled=True,
        ),
        axis=1,
    )
    hidden_state = (
        lax.dynamic_slice_in_dim(residual, first_col, slice_width, 1).astype(jnp.float32) + shared
    )
    squares = lax.psum(jnp.sum(hidden_state * hidden_state, axis=1), "tensor")
    gain_cols = lax.dynamic_slice_in_dim(norm_gain, first_col, slice_width, 0)
    normed = (
        hidden_state * lax.rsqrt(squares / model_width + 1e-06)[:, None] * gain_cols[None, :]
    ).astype(jnp.bfloat16)
    attended = hidden_state.astype(jnp.bfloat16)
    exp_here = expert_in.shape[0]
    sources = lax.axis_size("seq")
    experts = exp_here * sources
    top_k = expert_ids.shape[1]
    capacity = 2 * tok_rows * top_k // experts
    flat_ids = expert_ids.reshape(-1)
    onehot = (flat_ids[:, None] == jnp.arange(experts, dtype=jnp.int32)[None, :]).astype(jnp.int32)
    slot_index = jnp.sum((jnp.cumsum(onehot, axis=0) - 1) * onehot, axis=1)
    places = flat_ids * capacity + slot_index
    outgoing = (
        jnp.zeros((experts * capacity, slice_width), jnp.bfloat16)
        .at[places]
        .set(jnp.repeat(normed, top_k, axis=0))
    )
    incoming = lax.all_to_all(
        outgoing.reshape(sources, exp_here, capacity, slice_width),
        "seq",
        split_axis=0,
        concat_axis=0,
        tiled=True,
    )
    gate_up = jnp.einsum(
        "sjcd,jdgh->sjcgh",
        lax.all_gather(incoming, "tensor", axis=3, tiled=True),
        expert_in,
        preferred_element_type=jnp.float32,
    )
    hidden = (jax.nn.silu(gate_up[:, :, :, 0]) * gate_up[:, :, :, 1]).astype(jnp.bfloat16)
    group_terms = jnp.einsum(
        "sjch,jhd->sjcd", hidden, expert_out, preferred_element_type=jnp.float32
    )
    expert_rows_out = lax.psum_scatter(
        group_terms.astype(jnp.bfloat16), "tensor", scatter_dimension=3, tiled=True
    )
    returned = lax.all_to_all(expert_rows_out, "seq", split_axis=0, concat_axis=0, tiled=True)
    picked = returned.reshape(experts * capacity, slice_width)[places].reshape(
        tok_rows, top_k, slice_width
    )
    mixture = jnp.sum(gate_weights[:, :, None] * picked.astype(jnp.float32), axis=1)
    layer_out = (hidden_state + mixture).astype(jnp.bfloat16)
    return (attended, layer_out)


def solution(mesh):
    in_specs = (
        P("seq", "tensor"),
        P("seq", None, None, None),
        P("seq", None),
        P("seq", None),
        P("seq", None, None, None),
        P("seq"),
        P("seq", None),
        P("tensor", None),
        P(),
        P("seq", None),
        P("seq", None),
        P("seq", None, None, "tensor"),
        P("seq", "tensor", None),
    )
    out_specs = (P("seq", "tensor"), P("seq", "tensor"))
    return jax.shard_map(body, mesh=mesh, in_specs=in_specs, out_specs=out_specs, check_vma=False)
```

```python
import functools

import jax
import jax.numpy as jnp
from jax import lax
from jax.experimental import pallas as pl
from jax.experimental.pallas import tpu as pltpu
from jax.sharding import PartitionSpec as P


QH = 16
KVH = 4


NEG_SHIFT = -(2.0 ** 100)
TOKEN_BLOCKS = 4
STAT_ROWS = 16


def split3(x):
    hi = x.astype(jnp.bfloat16).astype(jnp.float32)
    rest = x - hi
    mid = rest.astype(jnp.bfloat16).astype(jnp.float32)
    lo = (rest - mid).astype(jnp.bfloat16).astype(jnp.float32)
    return hi, mid, lo


def shard_kernel(flag_ref, q_ref, k_ref, v_ref, o_ref, *, score_scale):
    step = pl.program_id(0)
    blocks, padded_rows, width = q_ref.shape
    rows = padded_rows - 1
    stat_rows = o_ref.shape[2] - rows
    owner = flag_ref[flag_ref.shape[0] - 1].astype(jnp.float32)
    kind = lax.broadcasted_iota(jnp.int32, (stat_rows, width), 0)
    blank = jnp.where(kind == 0, NEG_SHIFT, 0.0)
    for i in range(blocks):
        present = flag_ref[step * blocks + i] > 0

        @pl.when(present)
        def _():
            scores = (
                lax.dot_general(
                    q_ref[i, :rows, :], k_ref[...], (((1,), (1,)), ((), ())),
                    preferred_element_type=jnp.float32,
                )
                * score_scale
            )
            shift = jnp.max(scores, axis=1, keepdims=True)
            weights = jnp.exp(scores - shift)
            total = jnp.sum(weights, axis=1, keepdims=True)
            gathered = jnp.dot(
                weights.astype(jnp.bfloat16), v_ref[...], preferred_element_type=jnp.float32
            )
            o_ref[i, 0, :rows, :] = gathered.astype(jnp.bfloat16)
            lane = lax.broadcasted_iota(jnp.int32, (rows, width), 1)
            table = jnp.zeros((rows, width), jnp.float32)
            for col, part in enumerate(split3(shift) + split3(total)):
                table = jnp.where(lane == col, part, table)
            table = jnp.transpose(table)[:stat_rows, :]
            matching = q_ref[i, rows:, :].astype(jnp.float32) == owner
            o_ref[i, 0, rows:, :] = jnp.where(matching, table, blank).astype(jnp.bfloat16)

        @pl.when(jnp.logical_not(present))
        def _():
            o_ref[i, 0, :rows, :] = jnp.zeros((rows, width), jnp.bfloat16)
            o_ref[i, 0, rows:, :] = blank.astype(jnp.bfloat16)


def shard_attention(flags, gathered_q, keys, values, score_scale):
    sources, padded_rows, head_size = gathered_q.shape
    rows = padded_rows - 1
    tb = TOKEN_BLOCKS
    kernel = functools.partial(shard_kernel, score_scale=score_scale)
    grid_spec = pltpu.PrefetchScalarGridSpec(
        num_scalar_prefetch=1,
        grid=(sources // tb,),
        in_specs=[
            pl.BlockSpec((tb, padded_rows, head_size), lambda b, f: (b, 0, 0)),
            pl.BlockSpec(keys.shape, lambda b, f: (0, 0)),
            pl.BlockSpec(values.shape, lambda b, f: (0, 0)),
        ],
        out_specs=pl.BlockSpec((tb, 1, rows + STAT_ROWS, head_size), lambda b, f: (b, 0, 0, 0)),
    )
    return pl.pallas_call(
        kernel,
        grid_spec=grid_spec,
        out_shape=jax.ShapeDtypeStruct((sources, 1, rows + STAT_ROWS, head_size), jnp.bfloat16),
    )(flags, gathered_q, keys, values)


def layer(
    query,
    suffix_kv,
    segment_ids,
    request_prefix,
    prefix_kv,
    shard_prefix,
    residual,
    out_weight,
    norm_gain,
    expert_ids,
    gate_weights,
    expert_in,
    expert_out,
):
    tok_rows = query.shape[0]
    head_size = suffix_kv.shape[3]
    heads_here = query.shape[1] // head_size
    kv_head = lax.axis_index("tensor") * heads_here // (QH // KVH)
    score_scale = head_size ** (-0.5)
    queries = query.reshape(tok_rows, heads_here, head_size)
    segments = segment_ids[0]
    requests = jnp.arange(request_prefix.shape[1], dtype=jnp.int32)
    row_prefix = jnp.sum(
        jnp.where(segments[:, None] == requests[None, :], request_prefix[0][None, :], 0), axis=1
    )
    prefix_row = jnp.zeros((1, head_size), jnp.bfloat16).at[0, :tok_rows].set(
        row_prefix.astype(jnp.bfloat16)
    )
    sources = lax.axis_size("seq")
    own_cache = lax.dynamic_slice_in_dim(prefix_kv, kv_head, 1, 1)[:, 0]
    got_o, got_shift, got_total = [], [], []
    flags = None
    for head in range(heads_here):
        own_rows = jnp.concatenate(
            [query[:, head * head_size : (head + 1) * head_size], prefix_row], axis=0
        )
        gathered_q = lax.all_to_all(
            jnp.broadcast_to(own_rows[None], (sources,) + own_rows.shape),
            "seq", split_axis=0, concat_axis=0, tiled=True,
        )
        if flags is None:
            valid = gathered_q[:, tok_rows, :tok_rows] == shard_prefix[0].astype(jnp.bfloat16)
            flags = jnp.concatenate(
                [jnp.any(valid, axis=1).astype(jnp.int32), shard_prefix.astype(jnp.int32)]
            )
        outgoing = shard_attention(flags, gathered_q, own_cache[:, 0], own_cache[:, 1], score_scale)
        returned = lax.all_to_all(
            outgoing, "seq", split_axis=0, concat_axis=0, tiled=True
        )
        got_st = returned[:, 0, tok_rows:, :].astype(jnp.float32)
        got_o.append(returned[:, 0, :tok_rows, :].astype(jnp.float32))
        got_shift.append(got_st[:, 0] + got_st[:, 1] + got_st[:, 2])
        got_total.append(got_st[:, 3] + got_st[:, 4] + got_st[:, 5])
    got_o = jnp.stack(got_o, axis=1)
    got_shift = jnp.stack(got_shift, axis=1)
    got_total = jnp.stack(got_total, axis=1)

    own_suffix = lax.dynamic_slice_in_dim(suffix_kv, kv_head, 1, 1).reshape(tok_rows, 2, head_size)
    positions = jnp.arange(tok_rows)
    causal = (segments[:, None] == segments[None, :]) & (positions[None, :] <= positions[:, None])
    suf_scores = (
        jnp.einsum("rhd,kd->hrk", queries, own_suffix[:, 0], preferred_element_type=jnp.float32)
        * score_scale
    )
    suf_scores = jnp.where(causal[None], suf_scores, -jnp.inf)
    suf_shift = jnp.max(suf_scores, axis=2)
    suf_weights = jnp.exp(suf_scores - suf_shift[:, :, None])
    suf_total = jnp.sum(suf_weights, axis=2)
    suf_o = jnp.einsum(
        "hrk,kd->hrd", suf_weights.astype(jnp.bfloat16), own_suffix[:, 1],
        preferred_element_type=jnp.float32,
    )
    common = jnp.maximum(suf_shift, jnp.max(got_shift, axis=0))
    got_scale = jnp.exp(got_shift - common[None])
    suf_scale = jnp.exp(suf_shift - common)
    numer = jnp.sum(got_o * got_scale[..., None], axis=0) + suf_o * suf_scale[..., None]
    denom = jnp.sum(got_total * got_scale, axis=0) + suf_total * suf_scale
    attention = (
        jnp.transpose(numer / denom[..., None], (1, 0, 2))
        .reshape(tok_rows, heads_here * head_size)
        .astype(jnp.bfloat16)
    )
    projected = jnp.dot(attention, out_weight, preferred_element_type=jnp.float32)
    model_width = residual.shape[1]
    slice_width = model_width // lax.axis_size("tensor")
    first_col = lax.axis_index("tensor") * slice_width
    tensor_size = lax.axis_size("tensor")
    shared = jnp.sum(
        lax.all_to_all(
            projected.reshape(tok_rows, tensor_size, slice_width),
            "tensor", split_axis=1, concat_axis=1, tiled=True,
        ),
        axis=1,
    )
    hidden_state = (
        lax.dynamic_slice_in_dim(residual, first_col, slice_width, 1).astype(jnp.float32) + shared
    )
    squares = lax.psum(jnp.sum(hidden_state * hidden_state, axis=1), "tensor")
    gain_cols = lax.dynamic_slice_in_dim(norm_gain, first_col, slice_width, 0)
    normed = (
        hidden_state * lax.rsqrt(squares / model_width + 1e-06)[:, None] * gain_cols[None, :]
    ).astype(jnp.bfloat16)
    attended = hidden_state.astype(jnp.bfloat16)
    exp_here = expert_in.shape[0]
    sources = lax.axis_size("seq")
    experts = exp_here * sources
    top_k = expert_ids.shape[1]
    capacity = 2 * tok_rows * top_k // experts
    flat_ids = expert_ids.reshape(-1)
    onehot = (flat_ids[:, None] == jnp.arange(experts, dtype=jnp.int32)[None, :]).astype(jnp.int32)
    slot_index = jnp.sum((jnp.cumsum(onehot, axis=0) - 1) * onehot, axis=1)
    places = flat_ids * capacity + slot_index
    outgoing = (
        jnp.zeros((experts * capacity, slice_width), jnp.bfloat16)
        .at[places]
        .set(jnp.repeat(normed, top_k, axis=0))
    )
    incoming = lax.all_to_all(
        outgoing.reshape(sources, exp_here, capacity, slice_width),
        "seq",
        split_axis=0,
        concat_axis=0,
        tiled=True,
    )
    gate_up = jnp.einsum(
        "sjcd,jdgh->sjcgh",
        lax.all_gather(incoming, "tensor", axis=3, tiled=True),
        expert_in,
        preferred_element_type=jnp.float32,
    )
    hidden = (jax.nn.silu(gate_up[:, :, :, 0]) * gate_up[:, :, :, 1]).astype(jnp.bfloat16)
    group_terms = jnp.einsum(
        "sjch,jhd->sjcd", hidden, expert_out, preferred_element_type=jnp.float32
    )
    expert_rows_out = lax.psum_scatter(
        group_terms.astype(jnp.bfloat16), "tensor", scatter_dimension=3, tiled=True
    )
    returned = lax.all_to_all(expert_rows_out, "seq", split_axis=0, concat_axis=0, tiled=True)
    picked = returned.reshape(experts * capacity, slice_width)[places].reshape(
        tok_rows, top_k, slice_width
    )
    mixture = jnp.sum(gate_weights[:, :, None] * picked.astype(jnp.float32), axis=1)
    layer_out = (hidden_state + mixture).astype(jnp.bfloat16)
    return (attended, layer_out)


def solution(mesh):
    in_specs = (
        P("seq", "tensor"),
        P("seq", None, None, None),
        P("seq", None),
        P("seq", None),
        P("seq", None, None, None),
        P("seq"),
        P("seq", None),
        P("tensor", None),
        P(),
        P("seq", None),
        P("seq", None),
        P("seq", None, None, "tensor"),
        P("seq", "tensor", None),
    )
    out_specs = (P("seq", "tensor"), P("seq", "tensor"))
    return jax.shard_map(layer, mesh=mesh, in_specs=in_specs, out_specs=out_specs, check_vma=False)
```

```python
import functools

import jax
import jax.numpy as jnp
from jax import lax
from jax.experimental import pallas as pl
from jax.experimental.pallas import tpu as pltpu
from jax.sharding import PartitionSpec as P


QH = 16
KVH = 4


NEG_SHIFT = -(2.0 ** 100)
TOKEN_BLOCKS = 4
STAT_ROWS = 16


def split3(x):
    hi = x.astype(jnp.bfloat16).astype(jnp.float32)
    rest = x - hi
    mid = rest.astype(jnp.bfloat16).astype(jnp.float32)
    lo = (rest - mid).astype(jnp.bfloat16).astype(jnp.float32)
    return hi, mid, lo


def shard_kernel(flag_ref, q_ref, k_ref, v_ref, o_ref, *, score_scale):
    step = pl.program_id(0)
    blocks, padded_rows, width = q_ref.shape
    rows = padded_rows - 1
    stat_rows = o_ref.shape[2] - rows
    owner = flag_ref[flag_ref.shape[0] - 1].astype(jnp.float32)
    kind = lax.broadcasted_iota(jnp.int32, (stat_rows, width), 0)
    blank = jnp.where(kind == 0, NEG_SHIFT, 0.0)
    for i in range(blocks):
        present = flag_ref[step * blocks + i] > 0

        @pl.when(present)
        def _():
            scores = (
                lax.dot_general(
                    q_ref[i, :rows, :], k_ref[...], (((1,), (1,)), ((), ())),
                    preferred_element_type=jnp.float32,
                )
                * score_scale
            )
            shift = jnp.max(scores, axis=1, keepdims=True)
            weights = jnp.exp(scores - shift)
            total = jnp.sum(weights, axis=1, keepdims=True)
            gathered = jnp.dot(
                weights.astype(jnp.bfloat16), v_ref[...], preferred_element_type=jnp.float32
            )
            o_ref[i, 0, :rows, :] = gathered.astype(jnp.bfloat16)
            lane = lax.broadcasted_iota(jnp.int32, (rows, width), 1)
            table = jnp.zeros((rows, width), jnp.float32)
            for col, part in enumerate(split3(shift) + split3(total)):
                table = jnp.where(lane == col, part, table)
            table = jnp.transpose(table)[:stat_rows, :]
            matching = q_ref[i, rows:, :].astype(jnp.float32) == owner
            o_ref[i, 0, rows:, :] = jnp.where(matching, table, blank).astype(jnp.bfloat16)

        @pl.when(jnp.logical_not(present))
        def _():
            o_ref[i, 0, :rows, :] = jnp.zeros((rows, width), jnp.bfloat16)
            o_ref[i, 0, rows:, :] = blank.astype(jnp.bfloat16)


def shard_attention(flags, gathered_q, keys, values, score_scale):
    sources, padded_rows, head_size = gathered_q.shape
    rows = padded_rows - 1
    tb = TOKEN_BLOCKS
    kernel = functools.partial(shard_kernel, score_scale=score_scale)
    grid_spec = pltpu.PrefetchScalarGridSpec(
        num_scalar_prefetch=1,
        grid=(sources // tb,),
        in_specs=[
            pl.BlockSpec((tb, padded_rows, head_size), lambda b, f: (b, 0, 0)),
            pl.BlockSpec(keys.shape, lambda b, f: (0, 0)),
            pl.BlockSpec(values.shape, lambda b, f: (0, 0)),
        ],
        out_specs=pl.BlockSpec((tb, 1, rows + STAT_ROWS, head_size), lambda b, f: (b, 0, 0, 0)),
    )
    return pl.pallas_call(
        kernel,
        grid_spec=grid_spec,
        out_shape=jax.ShapeDtypeStruct((sources, 1, rows + STAT_ROWS, head_size), jnp.bfloat16),
    )(flags, gathered_q, keys, values)


def layer(
    query,
    suffix_kv,
    segment_ids,
    request_prefix,
    prefix_kv,
    shard_prefix,
    residual,
    out_weight,
    norm_gain,
    expert_ids,
    gate_weights,
    expert_in,
    expert_out,
):
    tok_rows = query.shape[0]
    head_size = suffix_kv.shape[3]
    heads_here = query.shape[1] // head_size
    kv_head = lax.axis_index("tensor") * heads_here // (QH // KVH)
    score_scale = head_size ** (-0.5)
    queries = query.reshape(tok_rows, heads_here, head_size)
    segments = segment_ids[0]
    requests = jnp.arange(request_prefix.shape[1], dtype=jnp.int32)
    row_prefix = jnp.sum(
        jnp.where(segments[:, None] == requests[None, :], request_prefix[0][None, :], 0), axis=1
    )
    prefix_row = jnp.zeros((1, head_size), jnp.bfloat16).at[0, :tok_rows].set(
        row_prefix.astype(jnp.bfloat16)
    )
    sources = lax.axis_size("seq")
    own_cache = lax.dynamic_slice_in_dim(prefix_kv, kv_head, 1, 1)[:, 0]
    got_o, got_shift, got_total = [], [], []
    flags = None
    for head in range(heads_here):
        own_rows = jnp.concatenate(
            [query[:, head * head_size : (head + 1) * head_size], prefix_row], axis=0
        )
        if head == 0:
            gathered_q = lax.all_to_all(
                jnp.broadcast_to(own_rows[None], (sources,) + own_rows.shape),
                "seq", split_axis=0, concat_axis=0, tiled=True,
            )
        else:
            gathered_q = lax.all_gather(own_rows, "seq", axis=0, tiled=False)
        if flags is None:
            valid = gathered_q[:, tok_rows, :tok_rows] == shard_prefix[0].astype(jnp.bfloat16)
            flags = jnp.concatenate(
                [jnp.any(valid, axis=1).astype(jnp.int32), shard_prefix.astype(jnp.int32)]
            )
        outgoing = shard_attention(flags, gathered_q, own_cache[:, 0], own_cache[:, 1], score_scale)
        returned = lax.all_to_all(
            outgoing, "seq", split_axis=0, concat_axis=0, tiled=True
        )
        got_st = returned[:, 0, tok_rows:, :].astype(jnp.float32)
        got_o.append(returned[:, 0, :tok_rows, :].astype(jnp.float32))
        got_shift.append(got_st[:, 0] + got_st[:, 1] + got_st[:, 2])
        got_total.append(got_st[:, 3] + got_st[:, 4] + got_st[:, 5])
    got_o = jnp.stack(got_o, axis=1)
    got_shift = jnp.stack(got_shift, axis=1)
    got_total = jnp.stack(got_total, axis=1)

    own_suffix = lax.dynamic_slice_in_dim(suffix_kv, kv_head, 1, 1).reshape(tok_rows, 2, head_size)
    positions = jnp.arange(tok_rows)
    causal = (segments[:, None] == segments[None, :]) & (positions[None, :] <= positions[:, None])
    suf_scores = (
        jnp.einsum("rhd,kd->hrk", queries, own_suffix[:, 0], preferred_element_type=jnp.float32)
        * score_scale
    )
    suf_scores = jnp.where(causal[None], suf_scores, -jnp.inf)
    suf_shift = jnp.max(suf_scores, axis=2)
    suf_weights = jnp.exp(suf_scores - suf_shift[:, :, None])
    suf_total = jnp.sum(suf_weights, axis=2)
    suf_o = jnp.einsum(
        "hrk,kd->hrd", suf_weights.astype(jnp.bfloat16), own_suffix[:, 1],
        preferred_element_type=jnp.float32,
    )
    common = jnp.maximum(suf_shift, jnp.max(got_shift, axis=0))
    got_scale = jnp.exp(got_shift - common[None])
    suf_scale = jnp.exp(suf_shift - common)
    numer = jnp.sum(got_o * got_scale[..., None], axis=0) + suf_o * suf_scale[..., None]
    denom = jnp.sum(got_total * got_scale, axis=0) + suf_total * suf_scale
    attention = (
        jnp.transpose(numer / denom[..., None], (1, 0, 2))
        .reshape(tok_rows, heads_here * head_size)
        .astype(jnp.bfloat16)
    )
    projected = jnp.dot(attention, out_weight, preferred_element_type=jnp.float32)
    model_width = residual.shape[1]
    slice_width = model_width // lax.axis_size("tensor")
    first_col = lax.axis_index("tensor") * slice_width
    tensor_size = lax.axis_size("tensor")
    shared = jnp.sum(
        lax.all_to_all(
            projected.reshape(tok_rows, tensor_size, slice_width),
            "tensor", split_axis=1, concat_axis=1, tiled=True,
        ),
        axis=1,
    )
    hidden_state = (
        lax.dynamic_slice_in_dim(residual, first_col, slice_width, 1).astype(jnp.float32) + shared
    )
    attended = hidden_state.astype(jnp.bfloat16)
    exp_here = expert_in.shape[0]
    sources = lax.axis_size("seq")
    experts = exp_here * sources
    top_k = expert_ids.shape[1]
    capacity = 2 * tok_rows * top_k // experts
    flat_ids = expert_ids.reshape(-1)
    onehot = (flat_ids[:, None] == jnp.arange(experts, dtype=jnp.int32)[None, :]).astype(jnp.int32)
    slot_index = jnp.sum((jnp.cumsum(onehot, axis=0) - 1) * onehot, axis=1)
    places = flat_ids * capacity + slot_index
    pick = places[:, None] == jnp.arange(experts * capacity, dtype=jnp.int32)[None, :]
    send_pick = jnp.any(pick.reshape(tok_rows, top_k, -1), axis=1).astype(jnp.bfloat16)
    outgoing = lax.dot_general(
        send_pick, attended, (((0,), (0,)), ((), ())), preferred_element_type=jnp.float32
    ).astype(jnp.bfloat16)
    incoming = lax.all_to_all(
        outgoing.reshape(sources, exp_here, capacity, slice_width),
        "seq",
        split_axis=0,
        concat_axis=0,
        tiled=True,
    )
    rows_in = lax.all_gather(incoming, "tensor", axis=3, tiled=True).astype(jnp.float32)
    mean_square = jnp.mean(rows_in * rows_in, axis=3, keepdims=True)
    normed = (rows_in * lax.rsqrt(mean_square + 1e-06) * norm_gain).astype(jnp.bfloat16)
    gate_up = jnp.einsum(
        "sjcd,jdgh->sjcgh",
        normed,
        expert_in,
        preferred_element_type=jnp.float32,
    )
    hidden = (jax.nn.silu(gate_up[:, :, :, 0]) * gate_up[:, :, :, 1]).astype(jnp.bfloat16)
    group_terms = jnp.einsum(
        "sjch,jhd->sjcd", hidden, expert_out, preferred_element_type=jnp.float32
    )
    expert_rows_out = lax.psum_scatter(
        group_terms.astype(jnp.bfloat16), "tensor", scatter_dimension=3, tiled=True
    )
    returned = lax.all_to_all(expert_rows_out, "seq", split_axis=0, concat_axis=0, tiled=True)
    picked = jnp.dot(
        pick.astype(jnp.bfloat16),
        returned.reshape(experts * capacity, slice_width),
        preferred_element_type=jnp.float32,
    ).reshape(tok_rows, top_k, slice_width)
    mixture = jnp.sum(gate_weights[:, :, None] * picked, axis=1)
    layer_out = (hidden_state + mixture).astype(jnp.bfloat16)
    return (attended, layer_out)


def solution(mesh):
    in_specs = (
        P("seq", "tensor"),
        P("seq", None, None, None),
        P("seq", None),
        P("seq", None),
        P("seq", None, None, None),
        P("seq"),
        P("seq", None),
        P("tensor", None),
        P(),
        P("seq", None),
        P("seq", None),
        P("seq", None, None, "tensor"),
        P("seq", "tensor", None),
    )
    out_specs = (P("seq", "tensor"), P("seq", "tensor"))
    return jax.shard_map(layer, mesh=mesh, in_specs=in_specs, out_specs=out_specs, check_vma=False)
```

```python
import functools

import jax
import jax.numpy as jnp
from jax import lax
from jax.experimental import pallas as pl
from jax.experimental.pallas import tpu as pltpu
from jax.sharding import PartitionSpec as P


QH = 16
KVH = 4


NEG_SHIFT = -(2.0 ** 100)
TOKEN_BLOCKS = 4
STAT_ROWS = 16


def split3(x):
    hi = x.astype(jnp.bfloat16).astype(jnp.float32)
    rest = x - hi
    mid = rest.astype(jnp.bfloat16).astype(jnp.float32)
    lo = (rest - mid).astype(jnp.bfloat16).astype(jnp.float32)
    return hi, mid, lo


def shard_kernel(flag_ref, q_ref, k_ref, v_ref, o_ref, *, score_scale):
    step = pl.program_id(0)
    blocks, padded_rows, width = q_ref.shape
    rows = padded_rows - 1
    stat_rows = o_ref.shape[2] - rows
    owner = flag_ref[flag_ref.shape[0] - 1].astype(jnp.float32)
    kind = lax.broadcasted_iota(jnp.int32, (stat_rows, width), 0)
    blank = jnp.where(kind == 0, NEG_SHIFT, 0.0)
    for i in range(blocks):
        present = flag_ref[step * blocks + i] > 0

        @pl.when(present)
        def _():
            scores = (
                lax.dot_general(
                    q_ref[i, :rows, :], k_ref[...], (((1,), (1,)), ((), ())),
                    preferred_element_type=jnp.float32,
                )
                * score_scale
            )
            shift = jnp.max(scores, axis=1, keepdims=True)
            weights = jnp.exp(scores - shift)
            total = jnp.sum(weights, axis=1, keepdims=True)
            gathered = jnp.dot(
                weights.astype(jnp.bfloat16), v_ref[...], preferred_element_type=jnp.float32
            )
            o_ref[i, 0, :rows, :] = gathered.astype(jnp.bfloat16)
            lane = lax.broadcasted_iota(jnp.int32, (rows, width), 1)
            table = jnp.zeros((rows, width), jnp.float32)
            for col, part in enumerate(split3(shift) + split3(total)):
                table = jnp.where(lane == col, part, table)
            table = jnp.transpose(table)[:stat_rows, :]
            matching = q_ref[i, rows:, :].astype(jnp.float32) == owner
            o_ref[i, 0, rows:, :] = jnp.where(matching, table, blank).astype(jnp.bfloat16)

        @pl.when(jnp.logical_not(present))
        def _():
            o_ref[i, 0, :rows, :] = jnp.zeros((rows, width), jnp.bfloat16)
            o_ref[i, 0, rows:, :] = blank.astype(jnp.bfloat16)


def shard_attention(flags, gathered_q, keys, values, score_scale):
    sources, padded_rows, head_size = gathered_q.shape
    rows = padded_rows - 1
    tb = TOKEN_BLOCKS
    kernel = functools.partial(shard_kernel, score_scale=score_scale)
    grid_spec = pltpu.PrefetchScalarGridSpec(
        num_scalar_prefetch=1,
        grid=(sources // tb,),
        in_specs=[
            pl.BlockSpec((tb, padded_rows, head_size), lambda b, f: (b, 0, 0)),
            pl.BlockSpec(keys.shape, lambda b, f: (0, 0)),
            pl.BlockSpec(values.shape, lambda b, f: (0, 0)),
        ],
        out_specs=pl.BlockSpec((tb, 1, rows + STAT_ROWS, head_size), lambda b, f: (b, 0, 0, 0)),
    )
    return pl.pallas_call(
        kernel,
        grid_spec=grid_spec,
        out_shape=jax.ShapeDtypeStruct((sources, 1, rows + STAT_ROWS, head_size), jnp.bfloat16),
    )(flags, gathered_q, keys, values)


def layer(
    query,
    suffix_kv,
    segment_ids,
    request_prefix,
    prefix_kv,
    shard_prefix,
    residual,
    out_weight,
    norm_gain,
    expert_ids,
    gate_weights,
    expert_in,
    expert_out,
):
    tok_rows = query.shape[0]
    head_size = suffix_kv.shape[3]
    heads_here = query.shape[1] // head_size
    kv_head = lax.axis_index("tensor") * heads_here // (QH // KVH)
    score_scale = head_size ** (-0.5)
    queries = query.reshape(tok_rows, heads_here, head_size)
    segments = segment_ids[0]
    requests = jnp.arange(request_prefix.shape[1], dtype=jnp.int32)
    row_prefix = jnp.sum(
        jnp.where(segments[:, None] == requests[None, :], request_prefix[0][None, :], 0), axis=1
    )
    prefix_row = jnp.zeros((1, head_size), jnp.bfloat16).at[0, :tok_rows].set(
        row_prefix.astype(jnp.bfloat16)
    )
    sources = lax.axis_size("seq")
    own_cache = lax.dynamic_slice_in_dim(prefix_kv, kv_head, 1, 1)[:, 0]
    own_suffix = lax.dynamic_slice_in_dim(suffix_kv, kv_head, 1, 1).reshape(tok_rows, 2, head_size)
    positions = jnp.arange(tok_rows)
    causal = (segments[:, None] == segments[None, :]) & (positions[None, :] <= positions[:, None])
    suf_scores = (
        jnp.einsum("rhd,kd->hrk", queries, own_suffix[:, 0], preferred_element_type=jnp.float32)
        * score_scale
    )
    suf_scores = jnp.where(causal[None], suf_scores, -jnp.inf)
    suf_shift = jnp.max(suf_scores, axis=2)
    suf_weights = jnp.exp(suf_scores - suf_shift[:, :, None])
    suf_total = jnp.sum(suf_weights, axis=2)
    suf_o = jnp.einsum(
        "hrk,kd->hrd", suf_weights.astype(jnp.bfloat16), own_suffix[:, 1],
        preferred_element_type=jnp.float32,
    )
    projected = None
    flags = None
    for head in range(heads_here):
        own_rows = jnp.concatenate(
            [query[:, head * head_size : (head + 1) * head_size], prefix_row], axis=0
        )
        gathered_q = lax.all_to_all(
            jnp.broadcast_to(own_rows[None], (sources,) + own_rows.shape),
            "seq", split_axis=0, concat_axis=0, tiled=True,
        )
        if flags is None:
            valid = gathered_q[:, tok_rows, :tok_rows] == shard_prefix[0].astype(jnp.bfloat16)
            flags = jnp.concatenate(
                [jnp.any(valid, axis=1).astype(jnp.int32), shard_prefix.astype(jnp.int32)]
            )
        outgoing = shard_attention(flags, gathered_q, own_cache[:, 0], own_cache[:, 1], score_scale)
        returned = lax.all_to_all(
            outgoing, "seq", split_axis=0, concat_axis=0, tiled=True
        )
        got_st = returned[:, 0, tok_rows:, :].astype(jnp.float32)
        got_o = returned[:, 0, :tok_rows, :].astype(jnp.float32)
        got_shift = got_st[:, 0] + got_st[:, 1] + got_st[:, 2]
        got_total = got_st[:, 3] + got_st[:, 4] + got_st[:, 5]
        common = jnp.maximum(suf_shift[head], jnp.max(got_shift, axis=0))
        got_scale = jnp.exp(got_shift - common[None])
        suf_scale = jnp.exp(suf_shift[head] - common)
        numer = jnp.sum(got_o * got_scale[..., None], axis=0) + suf_o[head] * suf_scale[:, None]
        denom = jnp.sum(got_total * got_scale, axis=0) + suf_total[head] * suf_scale
        attention = (numer / denom[:, None]).astype(jnp.bfloat16)
        part = jnp.dot(
            attention,
            out_weight[head * head_size : (head + 1) * head_size],
            preferred_element_type=jnp.float32,
        )
        projected = part if projected is None else projected + part
    model_width = residual.shape[1]
    slice_width = model_width // lax.axis_size("tensor")
    first_col = lax.axis_index("tensor") * slice_width
    tensor_size = lax.axis_size("tensor")
    shared = jnp.sum(
        lax.all_to_all(
            projected.astype(jnp.bfloat16).reshape(tok_rows, tensor_size, slice_width),
            "tensor", split_axis=1, concat_axis=1, tiled=True,
        ).astype(jnp.float32),
        axis=1,
    )
    hidden_state = (
        lax.dynamic_slice_in_dim(residual, first_col, slice_width, 1).astype(jnp.float32) + shared
    )
    attended = hidden_state.astype(jnp.bfloat16)
    exp_here = expert_in.shape[0]
    sources = lax.axis_size("seq")
    experts = exp_here * sources
    top_k = expert_ids.shape[1]
    capacity = 2 * tok_rows * top_k // experts
    flat_ids = expert_ids.reshape(-1)
    onehot = (flat_ids[:, None] == jnp.arange(experts, dtype=jnp.int32)[None, :]).astype(jnp.int32)
    slot_index = jnp.sum((jnp.cumsum(onehot, axis=0) - 1) * onehot, axis=1)
    places = flat_ids * capacity + slot_index
    pick = places[:, None] == jnp.arange(experts * capacity, dtype=jnp.int32)[None, :]
    send_pick = jnp.any(pick.reshape(tok_rows, top_k, -1), axis=1).astype(jnp.bfloat16)
    outgoing = lax.dot_general(
        send_pick, attended, (((0,), (0,)), ((), ())), preferred_element_type=jnp.float32
    ).astype(jnp.bfloat16)
    incoming = lax.all_to_all(
        outgoing.reshape(sources, exp_here, capacity, slice_width),
        "seq",
        split_axis=0,
        concat_axis=0,
        tiled=True,
    )
    rows_in = lax.all_gather(incoming, "tensor", axis=3, tiled=True).astype(jnp.float32)
    mean_square = jnp.mean(rows_in * rows_in, axis=3, keepdims=True)
    normed = (rows_in * lax.rsqrt(mean_square + 1e-06) * norm_gain).astype(jnp.bfloat16)
    gate_up = jnp.einsum(
        "sjcd,jdgh->sjcgh",
        normed,
        expert_in,
        preferred_element_type=jnp.float32,
    )
    hidden = (jax.nn.silu(gate_up[:, :, :, 0]) * gate_up[:, :, :, 1]).astype(jnp.bfloat16)
    group_terms = jnp.einsum(
        "sjch,jhd->sjcd", hidden, expert_out, preferred_element_type=jnp.float32
    )
    expert_rows_out = lax.psum_scatter(
        group_terms.astype(jnp.bfloat16), "tensor", scatter_dimension=3, tiled=True
    )
    returned = lax.all_to_all(expert_rows_out, "seq", split_axis=0, concat_axis=0, tiled=True)
    picked = jnp.dot(
        pick.astype(jnp.bfloat16),
        returned.reshape(experts * capacity, slice_width),
        preferred_element_type=jnp.float32,
    ).reshape(tok_rows, top_k, slice_width)
    mixture = jnp.sum(gate_weights[:, :, None] * picked, axis=1)
    layer_out = (hidden_state + mixture).astype(jnp.bfloat16)
    return (attended, layer_out)


def solution(mesh):
    in_specs = (
        P("seq", "tensor"),
        P("seq", None, None, None),
        P("seq", None),
        P("seq", None),
        P("seq", None, None, None),
        P("seq"),
        P("seq", None),
        P("tensor", None),
        P(),
        P("seq", None),
        P("seq", None),
        P("seq", None, None, "tensor"),
        P("seq", "tensor", None),
    )
    out_specs = (P("seq", "tensor"), P("seq", "tensor"))
    return jax.shard_map(layer, mesh=mesh, in_specs=in_specs, out_specs=out_specs, check_vma=False)
```

```python
import functools

import jax
import jax.numpy as jnp
from jax import lax
from jax.experimental import pallas as pl
from jax.experimental.pallas import tpu as pltpu
from jax.sharding import PartitionSpec as P


QH = 16
KVH = 4


NEG_SHIFT = -(2.0 ** 100)
TOKEN_BLOCKS = 4
STAT_ROWS = 16


def split3(x):
    hi = x.astype(jnp.bfloat16).astype(jnp.float32)
    rest = x - hi
    mid = rest.astype(jnp.bfloat16).astype(jnp.float32)
    lo = (rest - mid).astype(jnp.bfloat16).astype(jnp.float32)
    return hi, mid, lo


def shard_kernel(flag_ref, q_ref, p_ref, k_ref, v_ref, o_ref, *, score_scale):
    step = pl.program_id(0)
    blocks, rows, width = q_ref.shape
    stat_rows = o_ref.shape[2] - rows
    owner = flag_ref[flag_ref.shape[0] - 1].astype(jnp.float32)
    kind = lax.broadcasted_iota(jnp.int32, (stat_rows, width), 0)
    blank = jnp.where(kind == 0, NEG_SHIFT, 0.0)
    for i in range(blocks):
        present = flag_ref[step * blocks + i] > 0

        @pl.when(present)
        def _():
            scores = (
                lax.dot_general(
                    q_ref[i, :rows, :], k_ref[...], (((1,), (1,)), ((), ())),
                    preferred_element_type=jnp.float32,
                )
                * score_scale
            )
            shift = jnp.max(scores, axis=1, keepdims=True)
            weights = jnp.exp(scores - shift)
            total = jnp.sum(weights, axis=1, keepdims=True)
            gathered = jnp.dot(
                weights.astype(jnp.bfloat16), v_ref[...], preferred_element_type=jnp.float32
            )
            o_ref[i, 0, :rows, :] = gathered.astype(jnp.bfloat16)
            lane = lax.broadcasted_iota(jnp.int32, (rows, width), 1)
            table = jnp.zeros((rows, width), jnp.float32)
            for col, part in enumerate(split3(shift) + split3(total)):
                table = jnp.where(lane == col, part, table)
            table = jnp.transpose(table)[:stat_rows, :]
            matching = p_ref[i].astype(jnp.float32) == owner
            o_ref[i, 0, rows:, :] = jnp.where(matching, table, blank).astype(jnp.bfloat16)

        @pl.when(jnp.logical_not(present))
        def _():
            o_ref[i, 0, :rows, :] = jnp.zeros((rows, width), jnp.bfloat16)
            o_ref[i, 0, rows:, :] = blank.astype(jnp.bfloat16)


def shard_attention(flags, gathered_q, prefix_rows, keys, values, score_scale):
    sources = prefix_rows.shape[0]
    rows, head_size = gathered_q.shape[1] // 8 * 8, keys.shape[1]
    tb = TOKEN_BLOCKS
    kernel = functools.partial(shard_kernel, score_scale=score_scale)
    grid_spec = pltpu.PrefetchScalarGridSpec(
        num_scalar_prefetch=1,
        grid=(sources // tb,),
        in_specs=[
            pl.BlockSpec((tb, rows, head_size), lambda b, f: (b, 0, 0)),
            pl.BlockSpec((tb, 1, head_size), lambda b, f: (b, 0, 0)),
            pl.BlockSpec(keys.shape, lambda b, f: (0, 0)),
            pl.BlockSpec(values.shape, lambda b, f: (0, 0)),
        ],
        out_specs=pl.BlockSpec((tb, 1, rows + STAT_ROWS, head_size), lambda b, f: (b, 0, 0, 0)),
    )
    return pl.pallas_call(
        kernel,
        grid_spec=grid_spec,
        out_shape=jax.ShapeDtypeStruct((sources, 1, rows + STAT_ROWS, head_size), jnp.bfloat16),
    )(flags, gathered_q, prefix_rows, keys, values)


def layer(
    query,
    suffix_kv,
    segment_ids,
    request_prefix,
    prefix_kv,
    shard_prefix,
    residual,
    out_weight,
    norm_gain,
    expert_ids,
    gate_weights,
    expert_in,
    expert_out,
):
    tok_rows = query.shape[0]
    head_size = suffix_kv.shape[3]
    heads_here = query.shape[1] // head_size
    kv_head = lax.axis_index("tensor") * heads_here // (QH // KVH)
    score_scale = head_size ** (-0.5)
    queries = query.reshape(tok_rows, heads_here, head_size)
    segments = segment_ids[0]
    requests = jnp.arange(request_prefix.shape[1], dtype=jnp.int32)
    row_prefix = jnp.sum(
        jnp.where(segments[:, None] == requests[None, :], request_prefix[0][None, :], 0), axis=1
    )
    prefix_row = jnp.zeros((1, head_size), jnp.bfloat16).at[0, :tok_rows].set(
        row_prefix.astype(jnp.bfloat16)
    )
    sources = lax.axis_size("seq")
    own_cache = lax.dynamic_slice_in_dim(prefix_kv, kv_head, 1, 1)[:, 0]
    own_suffix = lax.dynamic_slice_in_dim(suffix_kv, kv_head, 1, 1).reshape(tok_rows, 2, head_size)
    positions = jnp.arange(tok_rows)
    causal = (segments[:, None] == segments[None, :]) & (positions[None, :] <= positions[:, None])
    suf_scores = (
        jnp.einsum("rhd,kd->hrk", queries, own_suffix[:, 0], preferred_element_type=jnp.float32)
        * score_scale
    )
    suf_scores = jnp.where(causal[None], suf_scores, -jnp.inf)
    suf_shift = jnp.max(suf_scores, axis=2)
    suf_weights = jnp.exp(suf_scores - suf_shift[:, :, None])
    suf_total = jnp.sum(suf_weights, axis=2)
    suf_o = jnp.einsum(
        "hrk,kd->hrd", suf_weights.astype(jnp.bfloat16), own_suffix[:, 1],
        preferred_element_type=jnp.float32,
    )
    projected = None
    flags = None
    for head in range(heads_here):
        own_rows = query[:, head * head_size : (head + 1) * head_size]
        if head == 0:
            own_rows = jnp.concatenate([own_rows, prefix_row], axis=0)
        gathered_q = lax.all_to_all(
            jnp.broadcast_to(own_rows[None], (sources,) + own_rows.shape),
            "seq", split_axis=0, concat_axis=0, tiled=True,
        )
        if flags is None:
            prefix_rows = gathered_q[:, tok_rows:, :]
            valid = gathered_q[:, tok_rows, :tok_rows] == shard_prefix[0].astype(jnp.bfloat16)
            flags = jnp.concatenate(
                [jnp.any(valid, axis=1).astype(jnp.int32), shard_prefix.astype(jnp.int32)]
            )
        outgoing = shard_attention(
            flags, gathered_q, prefix_rows, own_cache[:, 0], own_cache[:, 1], score_scale
        )
        returned = lax.all_to_all(
            outgoing, "seq", split_axis=0, concat_axis=0, tiled=True
        )
        got_st = returned[:, 0, tok_rows:, :].astype(jnp.float32)
        got_o = returned[:, 0, :tok_rows, :].astype(jnp.float32)
        got_shift = got_st[:, 0] + got_st[:, 1] + got_st[:, 2]
        got_total = got_st[:, 3] + got_st[:, 4] + got_st[:, 5]
        common = jnp.maximum(suf_shift[head], jnp.max(got_shift, axis=0))
        got_scale = jnp.exp(got_shift - common[None])
        suf_scale = jnp.exp(suf_shift[head] - common)
        numer = jnp.sum(got_o * got_scale[..., None], axis=0) + suf_o[head] * suf_scale[:, None]
        denom = jnp.sum(got_total * got_scale, axis=0) + suf_total[head] * suf_scale
        attention = (numer / denom[:, None]).astype(jnp.bfloat16)
        part = jnp.dot(
            attention,
            out_weight[head * head_size : (head + 1) * head_size],
            preferred_element_type=jnp.float32,
        )
        projected = part if projected is None else projected + part
    model_width = residual.shape[1]
    slice_width = model_width // lax.axis_size("tensor")
    first_col = lax.axis_index("tensor") * slice_width
    tensor_size = lax.axis_size("tensor")
    shared = jnp.sum(
        lax.all_to_all(
            projected.astype(jnp.bfloat16).reshape(tok_rows, tensor_size, slice_width),
            "tensor", split_axis=1, concat_axis=1, tiled=True,
        ).astype(jnp.float32),
        axis=1,
    )
    hidden_state = (
        lax.dynamic_slice_in_dim(residual, first_col, slice_width, 1).astype(jnp.float32) + shared
    )
    attended = hidden_state.astype(jnp.bfloat16)
    exp_here = expert_in.shape[0]
    sources = lax.axis_size("seq")
    experts = exp_here * sources
    top_k = expert_ids.shape[1]
    capacity = 2 * tok_rows * top_k // experts
    flat_ids = expert_ids.reshape(-1)
    onehot = (flat_ids[:, None] == jnp.arange(experts, dtype=jnp.int32)[None, :]).astype(jnp.int32)
    slot_index = jnp.sum((jnp.cumsum(onehot, axis=0) - 1) * onehot, axis=1)
    places = flat_ids * capacity + slot_index
    pick = places[:, None] == jnp.arange(experts * capacity, dtype=jnp.int32)[None, :]
    send_pick = jnp.any(pick.reshape(tok_rows, top_k, -1), axis=1).astype(jnp.bfloat16)
    outgoing = lax.dot_general(
        send_pick, attended, (((0,), (0,)), ((), ())), preferred_element_type=jnp.float32
    ).astype(jnp.bfloat16)
    incoming = lax.all_to_all(
        outgoing.reshape(sources, exp_here, capacity, slice_width),
        "seq",
        split_axis=0,
        concat_axis=0,
        tiled=True,
    )
    rows_in = lax.all_gather(incoming, "tensor", axis=3, tiled=True).astype(jnp.float32)
    mean_square = jnp.mean(rows_in * rows_in, axis=3, keepdims=True)
    normed = (rows_in * lax.rsqrt(mean_square + 1e-06) * norm_gain).astype(jnp.bfloat16)
    gate_up = jnp.einsum(
        "sjcd,jdgh->sjcgh",
        normed,
        expert_in,
        preferred_element_type=jnp.float32,
    )
    hidden = (jax.nn.silu(gate_up[:, :, :, 0]) * gate_up[:, :, :, 1]).astype(jnp.bfloat16)
    group_terms = jnp.einsum(
        "sjch,jhd->sjcd", hidden, expert_out, preferred_element_type=jnp.float32
    )
    expert_rows_out = lax.psum_scatter(
        group_terms.astype(jnp.bfloat16), "tensor", scatter_dimension=3, tiled=True
    )
    returned = lax.all_to_all(expert_rows_out, "seq", split_axis=0, concat_axis=0, tiled=True)
    picked = jnp.dot(
        pick.astype(jnp.bfloat16),
        returned.reshape(experts * capacity, slice_width),
        preferred_element_type=jnp.float32,
    ).reshape(tok_rows, top_k, slice_width)
    mixture = jnp.sum(gate_weights[:, :, None] * picked, axis=1)
    layer_out = (hidden_state + mixture).astype(jnp.bfloat16)
    return (attended, layer_out)


def solution(mesh):
    in_specs = (
        P("seq", "tensor"),
        P("seq", None, None, None),
        P("seq", None),
        P("seq", None),
        P("seq", None, None, None),
        P("seq"),
        P("seq", None),
        P("tensor", None),
        P(),
        P("seq", None),
        P("seq", None),
        P("seq", None, None, "tensor"),
        P("seq", "tensor", None),
    )
    out_specs = (P("seq", "tensor"), P("seq", "tensor"))
    return jax.shard_map(layer, mesh=mesh, in_specs=in_specs, out_specs=out_specs, check_vma=False)
```

```python
import functools

import jax
import jax.numpy as jnp
from jax import lax
from jax.experimental import pallas as pl
from jax.experimental.pallas import tpu as pltpu
from jax.sharding import PartitionSpec as P


QH = 16
KVH = 4


NEG_SHIFT = -(2.0 ** 100)
TOKEN_BLOCKS = 4
STAT_ROWS = 16


def split3(x):
    hi = x.astype(jnp.bfloat16).astype(jnp.float32)
    rest = x - hi
    mid = rest.astype(jnp.bfloat16).astype(jnp.float32)
    lo = (rest - mid).astype(jnp.bfloat16).astype(jnp.float32)
    return hi, mid, lo


def shard_kernel(flag_ref, q_ref, p_ref, k_ref, v_ref, o_ref, *, score_scale):
    step = pl.program_id(0)
    blocks, rows, width = q_ref.shape
    stat_rows = o_ref.shape[2] - rows
    owner = flag_ref[flag_ref.shape[0] - 1].astype(jnp.float32)
    kind = lax.broadcasted_iota(jnp.int32, (stat_rows, width), 0)
    blank = jnp.where(kind == 0, NEG_SHIFT, 0.0)
    for i in range(blocks):
        present = flag_ref[step * blocks + i] > 0

        @pl.when(present)
        def _():
            scores = (
                lax.dot_general(
                    q_ref[i, :rows, :], k_ref[...], (((1,), (1,)), ((), ())),
                    preferred_element_type=jnp.float32,
                )
                * score_scale
            )
            shift = jnp.max(scores, axis=1, keepdims=True)
            weights = jnp.exp(scores - shift)
            total = jnp.sum(weights, axis=1, keepdims=True)
            gathered = jnp.dot(
                weights.astype(jnp.bfloat16), v_ref[...], preferred_element_type=jnp.float32
            )
            o_ref[i, 0, :rows, :] = gathered.astype(jnp.bfloat16)
            lane = lax.broadcasted_iota(jnp.int32, (rows, width), 1)
            table = jnp.zeros((rows, width), jnp.float32)
            for col, part in enumerate(split3(shift) + split3(total)):
                table = jnp.where(lane == col, part, table)
            table = jnp.transpose(table)[:stat_rows, :]
            matching = p_ref[i].astype(jnp.float32) == owner
            o_ref[i, 0, rows:, :] = jnp.where(matching, table, blank).astype(jnp.bfloat16)

        @pl.when(jnp.logical_not(present))
        def _():
            o_ref[i, 0, :rows, :] = jnp.zeros((rows, width), jnp.bfloat16)
            o_ref[i, 0, rows:, :] = blank.astype(jnp.bfloat16)


def shard_attention(flags, gathered_q, prefix_rows, keys, values, score_scale):
    sources = prefix_rows.shape[0]
    rows, head_size = gathered_q.shape[1] // 8 * 8, keys.shape[1]
    tb = TOKEN_BLOCKS
    kernel = functools.partial(shard_kernel, score_scale=score_scale)
    grid_spec = pltpu.PrefetchScalarGridSpec(
        num_scalar_prefetch=1,
        grid=(sources // tb,),
        in_specs=[
            pl.BlockSpec((tb, rows, head_size), lambda b, f: (b, 0, 0)),
            pl.BlockSpec((tb, 1, head_size), lambda b, f: (b, 0, 0)),
            pl.BlockSpec(keys.shape, lambda b, f: (0, 0)),
            pl.BlockSpec(values.shape, lambda b, f: (0, 0)),
        ],
        out_specs=pl.BlockSpec((tb, 1, rows + STAT_ROWS, head_size), lambda b, f: (b, 0, 0, 0)),
    )
    return pl.pallas_call(
        kernel,
        grid_spec=grid_spec,
        out_shape=jax.ShapeDtypeStruct((sources, 1, rows + STAT_ROWS, head_size), jnp.bfloat16),
    )(flags, gathered_q, prefix_rows, keys, values)


def layer(
    query,
    suffix_kv,
    segment_ids,
    request_prefix,
    prefix_kv,
    shard_prefix,
    residual,
    out_weight,
    norm_gain,
    expert_ids,
    gate_weights,
    expert_in,
    expert_out,
):
    tok_rows = query.shape[0]
    head_size = suffix_kv.shape[3]
    heads_here = query.shape[1] // head_size
    kv_head = lax.axis_index("tensor") * heads_here // (QH // KVH)
    score_scale = head_size ** (-0.5)
    queries = query.reshape(tok_rows, heads_here, head_size)
    segments = segment_ids[0]
    requests = jnp.arange(request_prefix.shape[1], dtype=jnp.int32)
    row_prefix = jnp.sum(
        jnp.where(segments[:, None] == requests[None, :], request_prefix[0][None, :], 0), axis=1
    )
    routing = lax.all_gather(
        jnp.concatenate([segments, request_prefix[0]]), "seq", axis=0, tiled=False
    )
    all_requests = routing[:, tok_rows:]
    all_prefix = jnp.sum(
        jnp.where(
            routing[:, :tok_rows, None] == requests[None, None, :],
            all_requests[:, None, :],
            0,
        ),
        axis=2,
    )
    prefix_rows = all_prefix.astype(jnp.bfloat16)[:, None, :]
    valid = all_prefix == shard_prefix[0]
    flags = jnp.concatenate(
        [jnp.any(valid, axis=1).astype(jnp.int32), shard_prefix.astype(jnp.int32)]
    )
    sources = lax.axis_size("seq")
    own_cache = lax.dynamic_slice_in_dim(prefix_kv, kv_head, 1, 1)[:, 0]
    own_suffix = lax.dynamic_slice_in_dim(suffix_kv, kv_head, 1, 1).reshape(tok_rows, 2, head_size)
    positions = jnp.arange(tok_rows)
    causal = (segments[:, None] == segments[None, :]) & (positions[None, :] <= positions[:, None])
    suf_scores = (
        jnp.einsum("rhd,kd->hrk", queries, own_suffix[:, 0], preferred_element_type=jnp.float32)
        * score_scale
    )
    suf_scores = jnp.where(causal[None], suf_scores, -jnp.inf)
    suf_shift = jnp.max(suf_scores, axis=2)
    suf_weights = jnp.exp(suf_scores - suf_shift[:, :, None])
    suf_total = jnp.sum(suf_weights, axis=2)
    suf_o = jnp.einsum(
        "hrk,kd->hrd", suf_weights.astype(jnp.bfloat16), own_suffix[:, 1],
        preferred_element_type=jnp.float32,
    )
    projected = None
    for head in range(heads_here):
        own_rows = query[:, head * head_size : (head + 1) * head_size]
        gathered_q = lax.all_to_all(
            jnp.broadcast_to(own_rows[None], (sources,) + own_rows.shape),
            "seq", split_axis=0, concat_axis=0, tiled=True,
        )
        outgoing = shard_attention(
            flags, gathered_q, prefix_rows, own_cache[:, 0], own_cache[:, 1], score_scale
        )
        returned = lax.all_to_all(
            outgoing, "seq", split_axis=0, concat_axis=0, tiled=True
        )
        got_st = returned[:, 0, tok_rows:, :].astype(jnp.float32)
        got_o = returned[:, 0, :tok_rows, :].astype(jnp.float32)
        got_shift = got_st[:, 0] + got_st[:, 1] + got_st[:, 2]
        got_total = got_st[:, 3] + got_st[:, 4] + got_st[:, 5]
        common = jnp.maximum(suf_shift[head], jnp.max(got_shift, axis=0))
        got_scale = jnp.exp(got_shift - common[None])
        suf_scale = jnp.exp(suf_shift[head] - common)
        numer = jnp.sum(got_o * got_scale[..., None], axis=0) + suf_o[head] * suf_scale[:, None]
        denom = jnp.sum(got_total * got_scale, axis=0) + suf_total[head] * suf_scale
        attention = (numer / denom[:, None]).astype(jnp.bfloat16)
        part = jnp.dot(
            attention,
            out_weight[head * head_size : (head + 1) * head_size],
            preferred_element_type=jnp.float32,
        )
        projected = part if projected is None else projected + part
    model_width = residual.shape[1]
    slice_width = model_width // lax.axis_size("tensor")
    first_col = lax.axis_index("tensor") * slice_width
    tensor_size = lax.axis_size("tensor")
    shared = jnp.sum(
        lax.all_to_all(
            projected.astype(jnp.bfloat16).reshape(tok_rows, tensor_size, slice_width),
            "tensor", split_axis=1, concat_axis=1, tiled=True,
        ).astype(jnp.float32),
        axis=1,
    )
    hidden_state = (
        lax.dynamic_slice_in_dim(residual, first_col, slice_width, 1).astype(jnp.float32) + shared
    )
    attended = hidden_state.astype(jnp.bfloat16)
    exp_here = expert_in.shape[0]
    sources = lax.axis_size("seq")
    experts = exp_here * sources
    top_k = expert_ids.shape[1]
    capacity = 2 * tok_rows * top_k // experts
    flat_ids = expert_ids.reshape(-1)
    onehot = (flat_ids[:, None] == jnp.arange(experts, dtype=jnp.int32)[None, :]).astype(jnp.int32)
    slot_index = jnp.sum((jnp.cumsum(onehot, axis=0) - 1) * onehot, axis=1)
    places = flat_ids * capacity + slot_index
    pick = places[:, None] == jnp.arange(experts * capacity, dtype=jnp.int32)[None, :]
    send_pick = jnp.any(pick.reshape(tok_rows, top_k, -1), axis=1).astype(jnp.bfloat16)
    outgoing = lax.dot_general(
        send_pick, attended, (((0,), (0,)), ((), ())), preferred_element_type=jnp.float32
    ).astype(jnp.bfloat16)
    incoming = lax.all_to_all(
        outgoing.reshape(sources, exp_here, capacity, slice_width),
        "seq",
        split_axis=0,
        concat_axis=0,
        tiled=True,
    )
    rows_in = lax.all_gather(incoming, "tensor", axis=3, tiled=True).astype(jnp.float32)
    mean_square = jnp.mean(rows_in * rows_in, axis=3, keepdims=True)
    normed = (rows_in * lax.rsqrt(mean_square + 1e-06) * norm_gain).astype(jnp.bfloat16)
    gate_up = jnp.einsum(
        "sjcd,jdgh->sjcgh",
        normed,
        expert_in,
        preferred_element_type=jnp.float32,
    )
    hidden = (jax.nn.silu(gate_up[:, :, :, 0]) * gate_up[:, :, :, 1]).astype(jnp.bfloat16)
    group_terms = jnp.einsum(
        "sjch,jhd->sjcd", hidden, expert_out, preferred_element_type=jnp.float32
    )
    expert_rows_out = lax.psum_scatter(
        group_terms.astype(jnp.bfloat16), "tensor", scatter_dimension=3, tiled=True
    )
    returned = lax.all_to_all(expert_rows_out, "seq", split_axis=0, concat_axis=0, tiled=True)
    picked = jnp.dot(
        pick.astype(jnp.bfloat16),
        returned.reshape(experts * capacity, slice_width),
        preferred_element_type=jnp.float32,
    ).reshape(tok_rows, top_k, slice_width)
    mixture = jnp.sum(gate_weights[:, :, None] * picked, axis=1)
    layer_out = (hidden_state + mixture).astype(jnp.bfloat16)
    return (attended, layer_out)


def solution(mesh):
    in_specs = (
        P("seq", "tensor"),
        P("seq", None, None, None),
        P("seq", None),
        P("seq", None),
        P("seq", None, None, None),
        P("seq"),
        P("seq", None),
        P("tensor", None),
        P(),
        P("seq", None),
        P("seq", None),
        P("seq", None, None, "tensor"),
        P("seq", "tensor", None),
    )
    out_specs = (P("seq", "tensor"), P("seq", "tensor"))
    return jax.shard_map(layer, mesh=mesh, in_specs=in_specs, out_specs=out_specs, check_vma=False)
```
